32 devices in a mesh: snp: 16 (over z, x, core), smp: 2 (over y).
Axes of the slice: x: 2, y: 2, z: 4, core: 2. Of those that a mesh axis runs over, the one named last changes fastest.
Arguments:
- dosage: float32 [4096, 8192], P('smp', 'snp'), may hold values from 0 to 2
- reach: int32 [16], P('snp'), may hold values from 0 to 3, as said below
Outputs:
- ld_band: float32 [8192, 2048], P(('snp', 'smp'))
The draws below stay inside these ranges and needn't reach their ends.
Inputs may be any that keep to these rules, and one draw needn't show every extreme that they name: reach equals 3 at the last block.
All inputs are finite; a program needn't handle non-finite values.
Results may differ from the reference program's by a relative error of at most 0.008.
Values may be sent and summed in bfloat16 or wider, within the bound.
No kernel may reach another device: no remote copies, remote signals or barrier semaphores. Data moves between devices by JAX's collectives and lax.ppermute only.
A program may use at most 64 MiB of HBM per device.

```python
import jax
import jax.numpy as jnp
from jax import lax

BLOCK = 512
SMP_DEV = 2048
TAPS = 4
NBLK = 16
SNPS = 8192
SAMPLES = 4096
N_SMP = 2


def draw_dosage(key, part):
    key_freq = jax.random.fold_in(key, 11)
    key_noise = jax.random.fold_in(key, 12)
    key_offset = jax.random.fold_in(key, 14)
    key_gain = jax.random.fold_in(key, 15)
    key_sign = jax.random.fold_in(key, 16)
    freq = jax.random.uniform(key_freq, (1, SNPS), jnp.float32, 0.05, 0.5)
    noise = jax.random.normal(key_noise, (SAMPLES, SNPS), jnp.float32)
    column = jnp.arange(SNPS, dtype=jnp.int32)
    offsets = jax.random.randint(key_offset, (3, SNPS), 1, TAPS * BLOCK, jnp.int32)
    backward = column[None, :] - offsets
    source = jnp.where(backward >= 0, backward, column[None, :] + offsets) % SNPS
    signs = 2.0 * jax.random.randint(key_sign, (3, SNPS), 0, 2, jnp.int32).astype(jnp.float32) - 1.0
    gains = signs * jax.random.uniform(key_gain, (3, SNPS), jnp.float32, 0.5, 1.2)
    linked = noise + 0.7 * jnp.roll(noise, 1, axis=1)
    weight = jnp.full((SNPS,), 1.49, jnp.float32)
    for tag in range(3):
        linked = linked + gains[tag][None, :] * jnp.take(noise, source[tag], axis=1)
        weight = weight + gains[tag] * gains[tag]
    linked = linked / jnp.sqrt(weight)[None, :]
    rising = 1.0 + 2.0 * jnp.arange(SAMPLES, dtype=jnp.float32).reshape(SAMPLES, 1) / SAMPLES
    logit = jnp.log(freq / (1.0 - freq))
    return 2.0 * jax.nn.sigmoid(logit + rising * linked)


def draw_reach(key, part):
    values = jax.random.randint(jax.random.fold_in(key, 21), (NBLK,), 0, TAPS, jnp.int32)
    return values.at[NBLK - 1].set(TAPS - 1)


def setup_inputs(seed: int = 0) -> dict:
    streams_of = jax.random.split(jax.random.key(seed), 3)
    dosage = draw_dosage(jax.random.fold_in(streams_of[2], 71), 0)
    reach = draw_reach(jax.random.fold_in(streams_of[2], 71), 0)
    return {"dosage": dosage, "reach": reach}


def reference(dosage, reach):
    mean = lax.optimization_barrier(jnp.sum(dosage, axis=0)) / SAMPLES
    centered = dosage - mean
    var = lax.optimization_barrier(jnp.sum(centered * centered, axis=0)) / SAMPLES
    zed = (centered * lax.rsqrt(var + 1e-05)).astype(jnp.bfloat16)
    blocks = jnp.moveaxis(zed.reshape(N_SMP, SMP_DEV, NBLK, BLOCK), 2, 0)

    def one_block(index):
        own = blocks[index].astype(jnp.float32)
        tiles = []
        for dist in range(TAPS):
            other_index = index - dist
            other = blocks[jnp.maximum(other_index, 0)].astype(jnp.float32)
            partial_tile = jnp.einsum('ksa,ksb->kab', own, other)
            partial_tile = lax.optimization_barrier(partial_tile.astype(jnp.bfloat16)).astype(jnp.float32)
            tile = lax.optimization_barrier(jnp.sum(partial_tile, axis=0)) / SAMPLES
            keep = jnp.logical_and(dist <= reach[index], other_index >= 0)
            tiles.append(jnp.where(keep, tile, jnp.zeros_like(tile)))
        return jnp.concatenate(tiles, axis=1)
    result = lax.map(one_block, jnp.arange(NBLK, dtype=jnp.int32))
    return result.reshape(SNPS, TAPS * BLOCK)
```

```python
import jax
import jax.numpy as jnp
from jax import lax
from jax.sharding import PartitionSpec as P

TAPS = 4


def shifted(value, axis, steps):
    count = lax.axis_size(axis)
    first, last = (max(0, -steps), min(count, count - steps))
    return lax.ppermute(value, axis, [(source, source + steps) for source in range(first, last)])


def rotated(value, axis, steps):
    count = lax.axis_size(axis)
    return lax.ppermute(value, axis, [(source, (source + steps) % count) for source in range(count)])


def tile_term(standard, neighbour):
    return lax.dot_general(
        standard, neighbour, (((0,), (0,)), ((), ())), preferred_element_type=jnp.float32
    )


def local(dosage, reach):
    rows, width = dosage.shape
    n_smp = lax.axis_size("smp")
    samples = rows * n_smp
    me = lax.axis_index("smp")

    part_mean = jnp.sum(dosage, axis=0) / rows
    deviation = dosage - part_mean
    part_m2 = jnp.sum(deviation * deviation, axis=0)
    stats = jnp.stack([part_mean, part_m2])
    gathered = [stats] + [rotated(stats, "smp", s) for s in range(1, n_smp)]
    mean = gathered[0][0]
    for g in gathered[1:]:
        mean = mean + g[0]
    mean = mean / n_smp
    m2 = gathered[0][1]
    spread = (gathered[0][0] - mean) ** 2
    for g in gathered[1:]:
        m2 = m2 + g[1]
        spread = spread + (g[0] - mean) ** 2
    var = (m2 + rows * spread) / samples
    standard = ((dosage - mean) * lax.rsqrt(var + 1e-05)).astype(jnp.bfloat16)

    neighbours = [standard]
    previous = standard
    for dist in range(1, TAPS):
        previous = shifted(previous, "snp", 1)
        neighbours.append(previous)

    share = width // n_smp
    own_reach = reach[0]
    kept = []
    for dist in range(TAPS):
        partial = tile_term(standard, neighbours[dist]).astype(jnp.bfloat16)
        pieces = partial.reshape(n_smp, share, width)
        total = lax.dynamic_index_in_dim(pieces, me, 0, keepdims=False).astype(jnp.float32)
        for s in range(1, n_smp):
            outgoing = lax.dynamic_index_in_dim(pieces, (me + s) % n_smp, 0, keepdims=False)
            total = total + rotated(outgoing, "smp", s).astype(jnp.float32)
        tile = total / samples
        kept.append(jnp.where(dist <= own_reach, tile, jnp.zeros_like(tile)))
    return jnp.concatenate(kept, axis=1)


def solution(mesh):
    return jax.shard_map(
        local,
        mesh=mesh,
        in_specs=(P("smp", "snp"), P("snp")),
        out_specs=P(("snp", "smp"), None),
        check_vma=False,
    )
```

```python
import jax
import jax.numpy as jnp
from jax import lax
from jax.sharding import PartitionSpec as P

TAPS = 4
CHUNKS = 2


def shifted(value, axis, steps):
    count = lax.axis_size(axis)
    first, last = (max(0, -steps), min(count, count - steps))
    return lax.ppermute(value, axis, [(source, source + steps) for source in range(first, last)])


def rotated(value, axis, steps):
    count = lax.axis_size(axis)
    return lax.ppermute(value, axis, [(source, (source + steps) % count) for source in range(count)])


def chained(piece):
    out = []
    previous = piece
    for dist in range(1, TAPS):
        previous = shifted(previous, "snp", 1)
        out.append(previous)
    return out


def relayed(piece, count):
    def send(value, pairs):
        pairs = [(s, t) for s, t in pairs if 0 <= s < count and 0 <= t < count]
        return lax.ppermute(value, "snp", pairs)

    groups = range(0, count, 4)
    near = send(piece, [(b + i, b + i + 1) for b in groups for i in range(3)])
    far = send(piece, [p for b in groups for p in ((b, b + 3), (b + 1, b + 4), (b + 3, b + 6))])
    back = send(piece, [(b + 2, b) for b in groups])
    hop_a = send(back, [(b, b + 4) for b in groups])
    hop_b = send(far, [p for b in groups for p in ((b + 3, b + 2), (b + 2, b + 1))])
    hop_c = send(near, [(b + 2, b + 3) for b in groups])
    last_a = send(hop_b, [(b + 1, b) for b in groups])
    last_b = send(hop_a, [(b, b + 1) for b in groups])
    return [near + last_a, hop_a + hop_b + hop_c, far + last_b]


def tile_term(standard, neighbour):
    return lax.dot_general(
        standard, neighbour, (((0,), (0,)), ((), ())), preferred_element_type=jnp.float32
    )


def local(dosage, reach):
    rows, width = dosage.shape
    n_smp = lax.axis_size("smp")
    samples = rows * n_smp
    me = lax.axis_index("smp")

    part_mean = jnp.sum(dosage, axis=0) / rows
    deviation = dosage - part_mean
    part_m2 = jnp.sum(deviation * deviation, axis=0)
    stats = jnp.stack([part_mean, part_m2])
    gathered = [stats] + [rotated(stats, "smp", s) for s in range(1, n_smp)]
    mean = gathered[0][0]
    for g in gathered[1:]:
        mean = mean + g[0]
    mean = mean / n_smp
    m2 = gathered[0][1]
    spread = (gathered[0][0] - mean) ** 2
    for g in gathered[1:]:
        m2 = m2 + g[1]
        spread = spread + (g[0] - mean) ** 2
    var = (m2 + rows * spread) / samples
    standard = ((dosage - mean) * lax.rsqrt(var + 1e-05)).astype(jnp.bfloat16)

    chunks = CHUNKS if rows % (CHUNKS * 16) == 0 else 1
    step = rows // chunks
    pieces_of = [standard[c * step:(c + 1) * step] for c in range(chunks)]
    if lax.axis_size("snp") % 4 == 0:
        delivered = [relayed(piece, lax.axis_size("snp")) for piece in pieces_of]
    else:
        delivered = [chained(piece) for piece in pieces_of]

    share = width // n_smp
    own_reach = reach[0]
    kept = []
    for dist in range(TAPS):
        if dist == 0:
            partial = tile_term(standard, standard)
        else:
            partial = tile_term(pieces_of[0], delivered[0][dist - 1])
            for c in range(1, chunks):
                partial = partial + tile_term(pieces_of[c], delivered[c][dist - 1])
        partial = partial.astype(jnp.bfloat16)
        pieces = partial.reshape(n_smp, share, width)
        total = lax.dynamic_index_in_dim(pieces, me, 0, keepdims=False).astype(jnp.float32)
        for s in range(1, n_smp):
            outgoing = lax.dynamic_index_in_dim(pieces, (me + s) % n_smp, 0, keepdims=False)
            total = total + rotated(outgoing, "smp", s).astype(jnp.float32)
        tile = total / samples
        kept.append(jnp.where(dist <= own_reach, tile, jnp.zeros_like(tile)))
    return jnp.concatenate(kept, axis=1)


def solution(mesh):
    return jax.shard_map(
        local,
        mesh=mesh,
        in_specs=(P("smp", "snp"), P("snp")),
        out_specs=P(("snp", "smp"), None),
        check_vma=False,
    )
```

```python
import jax
import jax.numpy as jnp
from jax import lax
from jax.sharding import PartitionSpec as P

TAPS = 4
CHUNKS = 1


def shifted(value, axis, steps):
    count = lax.axis_size(axis)
    first, last = (max(0, -steps), min(count, count - steps))
    return lax.ppermute(value, axis, [(source, source + steps) for source in range(first, last)])


def rotated(value, axis, steps):
    count = lax.axis_size(axis)
    return lax.ppermute(value, axis, [(source, (source + steps) % count) for source in range(count)])


def chained(piece):
    out = []
    previous = piece
    for dist in range(1, TAPS):
        previous = shifted(previous, "snp", 1)
        out.append(previous)
    return out


def relayed(piece, count):
    def send(value, pairs):
        pairs = [(s, t) for s, t in pairs if 0 <= s < count and 0 <= t < count]
        return lax.ppermute(value, "snp", pairs)

    groups = range(0, count, 4)
    cross_one = send(piece, [(b + 1, b + 2) for b in groups])
    cross_three = send(piece, [(b, b + 3) for b in groups])
    up_three = send(piece, [p for b in groups for p in ((b + 1, b + 4), (b + 3, b + 6))])
    back = send(piece, [(b + 2, b) for b in groups])
    inner_one = send(piece, [p for b in groups for p in ((b, b + 1), (b + 2, b + 3))])
    up_two = send(back, [(b, b + 4) for b in groups])
    back_two = send(up_three, [(b + 2, b + 1) for b in groups])
    swap_a = send(cross_one, [(b + 2, b + 3) for b in groups])
    swap_b = send(cross_three, [(b + 3, b + 2) for b in groups])
    last_one = send(back_two, [(b + 1, b) for b in groups])
    last_three = send(up_two, [(b, b + 1) for b in groups])
    return [
        inner_one + cross_one + last_one,
        up_two + back_two + swap_a + swap_b,
        cross_three + up_three + last_three,
    ]


def tile_term(standard, neighbour):
    return lax.dot_general(
        standard, neighbour, (((0,), (0,)), ((), ())), preferred_element_type=jnp.float32
    )


def local(dosage, reach):
    rows, width = dosage.shape
    n_smp = lax.axis_size("smp")
    samples = rows * n_smp
    me = lax.axis_index("smp")

    part_mean = jnp.sum(dosage, axis=0) / rows
    deviation = dosage - part_mean
    part_m2 = jnp.sum(deviation * deviation, axis=0)
    stats = jnp.stack([part_mean, part_m2])
    gathered = [stats] + [rotated(stats, "smp", s) for s in range(1, n_smp)]
    mean = gathered[0][0]
    for g in gathered[1:]:
        mean = mean + g[0]
    mean = mean / n_smp
    m2 = gathered[0][1]
    spread = (gathered[0][0] - mean) ** 2
    for g in gathered[1:]:
        m2 = m2 + g[1]
        spread = spread + (g[0] - mean) ** 2
    var = (m2 + rows * spread) / samples
    standard = ((dosage - mean) * lax.rsqrt(var + 1e-05)).astype(jnp.bfloat16)

    chunks = CHUNKS if rows % (CHUNKS * 16) == 0 else 1
    step = rows // chunks
    pieces_of = [standard[c * step:(c + 1) * step] for c in range(chunks)]
    if lax.axis_size("snp") % 4 == 0:
        delivered = [relayed(piece, lax.axis_size("snp")) for piece in pieces_of]
    else:
        delivered = [chained(piece) for piece in pieces_of]

    share = width // n_smp
    own_reach = reach[0]
    kept = []
    for dist in range(TAPS):
        if dist == 0:
            partial = tile_term(standard, standard)
        else:
            partial = tile_term(pieces_of[0], delivered[0][dist - 1])
            for c in range(1, chunks):
                partial = partial + tile_term(pieces_of[c], delivered[c][dist - 1])
        partial = partial.astype(jnp.bfloat16)
        pieces = partial.reshape(n_smp, share, width)
        total = lax.dynamic_index_in_dim(pieces, me, 0, keepdims=False).astype(jnp.float32)
        for s in range(1, n_smp):
            outgoing = lax.dynamic_index_in_dim(pieces, (me + s) % n_smp, 0, keepdims=False)
            total = total + rotated(outgoing, "smp", s).astype(jnp.float32)
        tile = total / samples
        kept.append(jnp.where(dist <= own_reach, tile, jnp.zeros_like(tile)))
    return jnp.concatenate(kept, axis=1)


def solution(mesh):
    return jax.shard_map(
        local,
        mesh=mesh,
        in_specs=(P("smp", "snp"), P("snp")),
        out_specs=P(("snp", "smp"), None),
        check_vma=False,
    )
```

```python
import jax
import jax.numpy as jnp
from jax import lax
from jax.sharding import PartitionSpec as P

TAPS = 4


def shifted(value, axis, steps):
    count = lax.axis_size(axis)
    first, last = (max(0, -steps), min(count, count - steps))
    return lax.ppermute(value, axis, [(source, source + steps) for source in range(first, last)])


def rotated(value, axis, steps):
    count = lax.axis_size(axis)
    return lax.ppermute(value, axis, [(source, (source + steps) % count) for source in range(count)])


def chained(piece):
    out = []
    previous = piece
    for dist in range(1, TAPS):
        previous = shifted(previous, "snp", 1)
        out.append(previous)
    return out


def relayed(piece, count):
    def send(value, pairs):
        pairs = [(s, t) for s, t in pairs if 0 <= s < count and 0 <= t < count]
        return lax.ppermute(value, "snp", pairs)

    groups = range(0, count, 4)
    cross_one = send(piece, [(b + 1, b + 2) for b in groups])
    cross_three = send(piece, [(b, b + 3) for b in groups])
    up_three = send(piece, [p for b in groups for p in ((b + 1, b + 4), (b + 3, b + 6))])
    back = send(piece, [(b + 2, b) for b in groups])
    inner_one = send(piece, [p for b in groups for p in ((b, b + 1), (b + 2, b + 3))])
    inner_back = send(piece, [(b + 3, b + 2) for b in groups])
    up_two = send(back, [(b, b + 4) for b in groups])
    back_two = send(up_three, [(b + 2, b + 1) for b in groups])
    last_one = send(back_two, [(b + 1, b) for b in groups])
    last_three = send(up_two, [(b, b + 1) for b in groups])
    early = [inner_one + last_one, up_two + back_two, up_three + last_three]
    late = cross_one + cross_three
    partner = inner_back + inner_one
    return early, late, partner


def swap_partner(value, count):
    pairs = [p for b in range(0, count, 4) for p in ((b + 2, b + 3), (b + 3, b + 2))]
    return lax.ppermute(value, "snp", [(s, t) for s, t in pairs if t < count])


def tile_term(standard, neighbour):
    return lax.dot_general(
        standard, neighbour, (((0,), (0,)), ((), ())), preferred_element_type=jnp.float32
    )


def local(dosage, reach):
    rows, width = dosage.shape
    n_smp = lax.axis_size("smp")
    samples = rows * n_smp
    me = lax.axis_index("smp")

    part_mean = jnp.sum(dosage, axis=0) / rows
    deviation = dosage - part_mean
    part_m2 = jnp.sum(deviation * deviation, axis=0)
    stats = jnp.stack([part_mean, part_m2])
    gathered = [stats] + [rotated(stats, "smp", s) for s in range(1, n_smp)]
    mean = gathered[0][0]
    for g in gathered[1:]:
        mean = mean + g[0]
    mean = mean / n_smp
    m2 = gathered[0][1]
    spread = (gathered[0][0] - mean) ** 2
    for g in gathered[1:]:
        m2 = m2 + g[1]
        spread = spread + (g[0] - mean) ** 2
    var = (m2 + rows * spread) / samples
    standard = ((dosage - mean) * lax.rsqrt(var + 1e-05)).astype(jnp.bfloat16)

    count = lax.axis_size("snp")
    share = width // n_smp
    own_reach = reach[0]
    if count % 4 == 0:
        early, late, partner = relayed(standard, count)
        place = lax.axis_index("snp") % 4
        own_late = tile_term(standard, late)
        for_partner = swap_partner(tile_term(partner, late).astype(jnp.bfloat16), count)
        partials = [tile_term(standard, standard).astype(jnp.bfloat16)]
        partials.append(
            (tile_term(standard, early[0]) + jnp.where(place == 2, own_late, 0.0)).astype(jnp.bfloat16)
        )
        partials.append(tile_term(standard, early[1]).astype(jnp.bfloat16) + for_partner)
        partials.append(
            (tile_term(standard, early[2]) + jnp.where(place == 3, own_late, 0.0)).astype(jnp.bfloat16)
        )
    else:
        neighbours = [standard] + chained(standard)
        partials = [tile_term(standard, nb).astype(jnp.bfloat16) for nb in neighbours]

    kept = []
    for dist in range(TAPS):
        pieces = partials[dist].reshape(n_smp, share, width)
        total = lax.dynamic_index_in_dim(pieces, me, 0, keepdims=False).astype(jnp.float32)
        for s in range(1, n_smp):
            outgoing = lax.dynamic_index_in_dim(pieces, (me + s) % n_smp, 0, keepdims=False)
            total = total + rotated(outgoing, "smp", s).astype(jnp.float32)
        tile = total / samples
        kept.append(jnp.where(dist <= own_reach, tile, jnp.zeros_like(tile)))
    return jnp.concatenate(kept, axis=1)


def solution(mesh):
    return jax.shard_map(
        local,
        mesh=mesh,
        in_specs=(P("smp", "snp"), P("snp")),
        out_specs=P(("snp", "smp"), None),
        check_vma=False,
    )
```

```python
import jax
import jax.numpy as jnp
from jax import lax
from jax.sharding import PartitionSpec as P

TAPS = 4


def shifted(value, axis, steps):
    count = lax.axis_size(axis)
    first, last = (max(0, -steps), min(count, count - steps))
    return lax.ppermute(value, axis, [(source, source + steps) for source in range(first, last)])


def rotated(value, axis, steps):
    count = lax.axis_size(axis)
    return lax.ppermute(value, axis, [(source, (source + steps) % count) for source in range(count)])


def chained(piece):
    out = []
    previous = piece
    for dist in range(1, TAPS):
        previous = shifted(previous, "snp", 1)
        out.append(previous)
    return out


def relayed(standard, count, place):
    def send(value, pairs):
        pairs = [(s, t) for s, t in pairs if 0 <= s < count and 0 <= t < count]
        return lax.ppermute(value, "snp", pairs)

    def pairs_of(*steps):
        return [(b + s, b + t) for b in range(0, count, 4) for s, t in steps]

    cross = send(standard, pairs_of((1, 2), (0, 3)))
    fast_a = send(standard, pairs_of((0, 1), (2, 3), (1, 4), (3, 6)))
    fast_b = send(standard, pairs_of((2, 1), (3, 2), (1, 0)))
    relay = send(jnp.where(place == 1, fast_b, fast_a), pairs_of((1, 4), (2, 1)))
    lhs = jnp.where(place % 2 == 0, fast_b, fast_a)
    rhs = jnp.where(place < 2, relay, cross)
    handed = send(tile_term(lhs, rhs).astype(jnp.bfloat16), pairs_of((0, 1), (1, 0), (2, 3), (3, 2)))
    with_a = tile_term(standard, fast_a).astype(jnp.bfloat16)
    with_relay = tile_term(standard, relay).astype(jnp.bfloat16)
    with_cross = tile_term(standard, cross).astype(jnp.bfloat16)
    one = jnp.where(place == 0, handed, jnp.where(place == 2, with_cross, with_a))
    two = jnp.where(place < 2, with_relay, handed)
    three = jnp.where(place == 1, handed, jnp.where(place == 3, with_cross, with_a))
    return [one, two, three]


def tile_term(standard, neighbour):
    return lax.dot_general(
        standard, neighbour, (((0,), (0,)), ((), ())), preferred_element_type=jnp.float32
    )


def local(dosage, reach):
    rows, width = dosage.shape
    n_smp = lax.axis_size("smp")
    samples = rows * n_smp
    me = lax.axis_index("smp")

    part_mean = jnp.sum(dosage, axis=0) / rows
    deviation = dosage - part_mean
    part_m2 = jnp.sum(deviation * deviation, axis=0)
    stats = jnp.stack([part_mean, part_m2])
    gathered = [stats] + [rotated(stats, "smp", s) for s in range(1, n_smp)]
    mean = gathered[0][0]
    for g in gathered[1:]:
        mean = mean + g[0]
    mean = mean / n_smp
    m2 = gathered[0][1]
    spread = (gathered[0][0] - mean) ** 2
    for g in gathered[1:]:
        m2 = m2 + g[1]
        spread = spread + (g[0] - mean) ** 2
    var = (m2 + rows * spread) / samples
    standard = ((dosage - mean) * lax.rsqrt(var + 1e-05)).astype(jnp.bfloat16)

    count = lax.axis_size("snp")
    share = width // n_smp
    own_reach = reach[0]
    first = tile_term(standard, standard).astype(jnp.bfloat16)
    if count % 4 == 0:
        rest = relayed(standard, count, lax.axis_index("snp") % 4)
    else:
        rest = [tile_term(standard, nb).astype(jnp.bfloat16) for nb in chained(standard)]

    def exchanged(partial):
        pieces = partial.reshape(partial.shape[:-2] + (n_smp, share, width))
        axis = pieces.ndim - 3
        total = lax.dynamic_index_in_dim(pieces, me, axis, keepdims=False).astype(jnp.float32)
        for s in range(1, n_smp):
            outgoing = lax.dynamic_index_in_dim(pieces, (me + s) % n_smp, axis, keepdims=False)
            total = total + rotated(outgoing, "smp", s).astype(jnp.float32)
        return total

    totals = [exchanged(first)] + list(exchanged(jnp.stack(rest)))
    kept = []
    for dist in range(TAPS):
        tile = totals[dist] / samples
        kept.append(jnp.where(dist <= own_reach, tile, jnp.zeros_like(tile)))
    return jnp.concatenate(kept, axis=1)


def solution(mesh):
    return jax.shard_map(
        local,
        mesh=mesh,
        in_specs=(P("smp", "snp"), P("snp")),
        out_specs=P(("snp", "smp"), None),
        check_vma=False,
    )
```

```python
import jax
import jax.numpy as jnp
from jax import lax
from jax.sharding import PartitionSpec as P

TAPS = 4


def shifted(value, axis, steps):
    count = lax.axis_size(axis)
    first, last = (max(0, -steps), min(count, count - steps))
    return lax.ppermute(value, axis, [(source, source + steps) for source in range(first, last)])


def rotated(value, axis, steps):
    count = lax.axis_size(axis)
    return lax.ppermute(value, axis, [(source, (source + steps) % count) for source in range(count)])


def chained(piece):
    out = []
    previous = piece
    for dist in range(1, TAPS):
        previous = shifted(previous, "snp", 1)
        out.append(previous)
    return out


def relayed(standard, count, place):
    def send(value, pairs):
        pairs = [(s, t) for s, t in pairs if 0 <= s < count and 0 <= t < count]
        return lax.ppermute(value, "snp", pairs)

    def pairs_of(*steps):
        return [(b + s, b + t) for b in range(0, count, 4) for s, t in steps]

    cross = send(standard, pairs_of((1, 2), (0, 3)))
    fast_a = send(standard, pairs_of((0, 1), (2, 3), (1, 4), (3, 6)))
    fast_b = send(standard, pairs_of((2, 1), (3, 2), (1, 0)))
    relay = send(fast_b, pairs_of((1, 4))) + send(fast_a, pairs_of((2, 1)))
    lhs = jnp.where(place % 2 == 0, fast_b, fast_a)
    rhs = jnp.where(place < 2, relay, cross)
    handed = send(tile_term(lhs, rhs).astype(jnp.bfloat16), pairs_of((0, 1), (1, 0), (2, 3), (3, 2)))
    with_a = tile_term(standard, fast_a).astype(jnp.bfloat16)
    with_relay = tile_term(standard, relay).astype(jnp.bfloat16)
    with_cross = tile_term(standard, cross).astype(jnp.bfloat16)
    one = jnp.where(place == 0, handed, jnp.where(place == 2, with_cross, with_a))
    two = jnp.where(place < 2, with_relay, handed)
    three = jnp.where(place == 1, handed, jnp.where(place == 3, with_cross, with_a))
    return [one, two, three]


def tile_term(standard, neighbour):
    return lax.dot_general(
        standard, neighbour, (((0,), (0,)), ((), ())), preferred_element_type=jnp.float32
    )


def local(dosage, reach):
    rows, width = dosage.shape
    n_smp = lax.axis_size("smp")
    samples = rows * n_smp
    me = lax.axis_index("smp")

    part_mean = jnp.sum(dosage, axis=0) / rows
    deviation = dosage - part_mean
    part_m2 = jnp.sum(deviation * deviation, axis=0)
    stats = jnp.stack([part_mean, part_m2])
    gathered = [stats] + [rotated(stats, "smp", s) for s in range(1, n_smp)]
    mean = gathered[0][0]
    for g in gathered[1:]:
        mean = mean + g[0]
    mean = mean / n_smp
    m2 = gathered[0][1]
    spread = (gathered[0][0] - mean) ** 2
    for g in gathered[1:]:
        m2 = m2 + g[1]
        spread = spread + (g[0] - mean) ** 2
    var = (m2 + rows * spread) / samples
    standard = ((dosage - mean) * lax.rsqrt(var + 1e-05)).astype(jnp.bfloat16)

    count = lax.axis_size("snp")
    share = width // n_smp
    own_reach = reach[0]
    first = tile_term(standard, standard).astype(jnp.bfloat16)
    if count % 4 == 0:
        rest = relayed(standard, count, lax.axis_index("snp") % 4)
    else:
        rest = [tile_term(standard, nb).astype(jnp.bfloat16) for nb in chained(standard)]

    def exchanged(partial):
        pieces = partial.reshape(partial.shape[:-2] + (n_smp, share, width))
        axis = pieces.ndim - 3
        total = lax.dynamic_index_in_dim(pieces, me, axis, keepdims=False).astype(jnp.float32)
        for s in range(1, n_smp):
            outgoing = lax.dynamic_index_in_dim(pieces, (me + s) % n_smp, axis, keepdims=False)
            total = total + rotated(outgoing, "smp", s).astype(jnp.float32)
        return total

    totals = list(exchanged(jnp.stack([first] + rest)))
    kept = []
    for dist in range(TAPS):
        tile = totals[dist] / samples
        kept.append(jnp.where(dist <= own_reach, tile, jnp.zeros_like(tile)))
    return jnp.concatenate(kept, axis=1)


def solution(mesh):
    return jax.shard_map(
        local,
        mesh=mesh,
        in_specs=(P("smp", "snp"), P("snp")),
        out_specs=P(("snp", "smp"), None),
        check_vma=False,
    )
```

```python
import jax
import jax.numpy as jnp
from jax import lax
from jax.sharding import PartitionSpec as P

TAPS = 4


def shifted(value, axis, steps):
    count = lax.axis_size(axis)
    first, last = (max(0, -steps), min(count, count - steps))
    return lax.ppermute(value, axis, [(source, source + steps) for source in range(first, last)])


def rotated(value, axis, steps):
    count = lax.axis_size(axis)
    return lax.ppermute(value, axis, [(source, (source + steps) % count) for source in range(count)])


def chained(piece):
    out = []
    previous = piece
    for dist in range(1, TAPS):
        previous = shifted(previous, "snp", 1)
        out.append(previous)
    return out


def relayed(standard, count, place):
    def send(value, pairs):
        pairs = [(s, t) for s, t in pairs if 0 <= s < count and 0 <= t < count]
        return lax.ppermute(value, "snp", pairs)

    def pairs_of(*steps):
        return [(b + s, b + t) for b in range(0, count, 4) for s, t in steps]

    cross = send(standard, pairs_of((1, 2), (0, 3)))
    fast_a = send(standard, pairs_of((0, 1), (2, 3), (1, 4), (3, 6)))
    fast_b = send(standard, pairs_of((2, 1), (3, 2), (1, 0)))
    relay = send(fast_b, pairs_of((1, 4))) + send(fast_a, pairs_of((2, 1)))
    lhs = jnp.where(place % 2 == 0, fast_b, fast_a)
    rhs = jnp.where(place < 2, relay, cross)
    handed = send(tile_term(lhs, rhs).astype(jnp.bfloat16), pairs_of((0, 1), (1, 0), (2, 3), (3, 2)))
    with_a = tile_term(standard, fast_a).astype(jnp.bfloat16)
    with_relay = tile_term(standard, relay).astype(jnp.bfloat16)
    with_cross = tile_term(standard, cross).astype(jnp.bfloat16)
    return with_a, jnp.where(place < 2, with_relay, with_cross), handed


def tile_term(standard, neighbour):
    return lax.dot_general(
        standard, neighbour, (((0,), (0,)), ((), ())), preferred_element_type=jnp.float32
    )


def local(dosage, reach):
    rows, width = dosage.shape
    n_smp = lax.axis_size("smp")
    samples = rows * n_smp
    me = lax.axis_index("smp")

    part_mean = jnp.sum(dosage, axis=0) / rows
    deviation = dosage - part_mean
    part_m2 = jnp.sum(deviation * deviation, axis=0)
    stats = jnp.stack([part_mean, part_m2])
    gathered = [stats] + [rotated(stats, "smp", s) for s in range(1, n_smp)]
    mean = gathered[0][0]
    for g in gathered[1:]:
        mean = mean + g[0]
    mean = mean / n_smp
    m2 = gathered[0][1]
    spread = (gathered[0][0] - mean) ** 2
    for g in gathered[1:]:
        m2 = m2 + g[1]
        spread = spread + (g[0] - mean) ** 2
    var = (m2 + rows * spread) / samples
    standard = ((dosage - mean) * lax.rsqrt(var + 1e-05)).astype(jnp.bfloat16)

    count = lax.axis_size("snp")
    share = width // n_smp
    own_reach = reach[0]
    first = tile_term(standard, standard).astype(jnp.bfloat16)

    def exchanged(partial):
        pieces = partial.reshape(partial.shape[:-2] + (n_smp, share, width))
        axis = pieces.ndim - 3
        total = lax.dynamic_index_in_dim(pieces, me, axis, keepdims=False).astype(jnp.float32)
        for s in range(1, n_smp):
            outgoing = lax.dynamic_index_in_dim(pieces, (me + s) % n_smp, axis, keepdims=False)
            total = total + rotated(outgoing, "smp", s).astype(jnp.float32)
        return total

    if count % 4 == 0:
        place = lax.axis_index("snp") % 4
        with_a, own_late, handed = relayed(standard, count, place)
        early = exchanged(jnp.stack([first, with_a]))
        late = exchanged(jnp.stack([own_late, handed]))
        totals = [
            early[0],
            jnp.where(place == 0, late[1], jnp.where(place == 2, late[0], early[1])),
            jnp.where(place < 2, late[0], late[1]),
            jnp.where(place == 1, late[1], jnp.where(place == 3, late[0], early[1])),
        ]
    else:
        rest = [tile_term(standard, nb).astype(jnp.bfloat16) for nb in chained(standard)]
        totals = list(exchanged(jnp.stack([first] + rest)))
    kept = []
    for dist in range(TAPS):
        tile = totals[dist] / samples
        kept.append(jnp.where(dist <= own_reach, tile, jnp.zeros_like(tile)))
    return jnp.concatenate(kept, axis=1)


def solution(mesh):
    return jax.shard_map(
        local,
        mesh=mesh,
        in_specs=(P("smp", "snp"), P("snp")),
        out_specs=P(("snp", "smp"), None),
        check_vma=False,
    )
```

```python
import jax
import jax.numpy as jnp
from jax import lax
from jax.sharding import PartitionSpec as P

TAPS = 4


def shifted(value, axis, steps):
    count = lax.axis_size(axis)
    first, last = (max(0, -steps), min(count, count - steps))
    return lax.ppermute(value, axis, [(source, source + steps) for source in range(first, last)])


def rotated(value, axis, steps):
    count = lax.axis_size(axis)
    return lax.ppermute(value, axis, [(source, (source + steps) % count) for source in range(count)])


def chained(piece):
    out = []
    previous = piece
    for dist in range(1, TAPS):
        previous = shifted(previous, "snp", 1)
        out.append(previous)
    return out


def relayed(standard, count, place):
    def send(value, pairs):
        pairs = [(s, t) for s, t in pairs if 0 <= s < count and 0 <= t < count]
        return lax.ppermute(value, "snp", pairs)

    def pairs_of(*steps):
        return [(b + s, b + t) for b in range(0, count, 4) for s, t in steps]

    cross = send(standard, pairs_of((1, 2), (0, 3)))
    fast_a = send(standard, pairs_of((0, 1), (2, 3), (1, 4), (3, 6)))
    fast_b = send(standard, pairs_of((2, 1), (3, 2), (1, 0)))
    relay = send(fast_b, pairs_of((1, 4))) + send(fast_a, pairs_of((2, 1)))
    lhs = jnp.where(place % 2 == 0, fast_b, fast_a)
    rhs = relay + cross
    handed = send(tile_term(lhs, rhs).astype(jnp.bfloat16), pairs_of((0, 1), (1, 0), (2, 3), (3, 2)))
    with_a = tile_term(standard, fast_a).astype(jnp.bfloat16)
    own_late = tile_term(standard, rhs).astype(jnp.bfloat16)
    return with_a, own_late, handed


def tile_term(standard, neighbour):
    return lax.dot_general(
        standard, neighbour, (((0,), (0,)), ((), ())), preferred_element_type=jnp.float32
    )


def local(dosage, reach):
    rows, width = dosage.shape
    n_smp = lax.axis_size("smp")
    samples = rows * n_smp
    me = lax.axis_index("smp")

    part_mean = jnp.sum(dosage, axis=0) / rows
    deviation = dosage - part_mean
    part_m2 = jnp.sum(deviation * deviation, axis=0)
    stats = jnp.stack([part_mean, part_m2])
    gathered = [stats] + [rotated(stats, "smp", s) for s in range(1, n_smp)]
    mean = gathered[0][0]
    for g in gathered[1:]:
        mean = mean + g[0]
    mean = mean / n_smp
    m2 = gathered[0][1]
    spread = (gathered[0][0] - mean) ** 2
    for g in gathered[1:]:
        m2 = m2 + g[1]
        spread = spread + (g[0] - mean) ** 2
    var = (m2 + rows * spread) / samples
    standard = ((dosage - mean) * lax.rsqrt(var + 1e-05)).astype(jnp.bfloat16)

    count = lax.axis_size("snp")
    share = width // n_smp
    own_reach = reach[0]
    first = tile_term(standard, standard).astype(jnp.bfloat16)

    def exchanged(partial):
        pieces = partial.reshape(partial.shape[:-2] + (n_smp, share, width))
        axis = pieces.ndim - 3
        total = lax.dynamic_index_in_dim(pieces, me, axis, keepdims=False).astype(jnp.float32)
        for s in range(1, n_smp):
            outgoing = lax.dynamic_index_in_dim(pieces, (me + s) % n_smp, axis, keepdims=False)
            total = total + rotated(outgoing, "smp", s).astype(jnp.float32)
        return total

    if count % 4 == 0:
        place = lax.axis_index("snp") % 4
        with_a, own_late, handed = relayed(standard, count, place)
        early = exchanged(jnp.stack([first, with_a]))
        late = [exchanged(own_late), exchanged(handed)]
        totals = [
            early[0],
            jnp.where(place == 0, late[1], jnp.where(place == 2, late[0], early[1])),
            jnp.where(place < 2, late[0], late[1]),
            jnp.where(place == 1, late[1], jnp.where(place == 3, late[0], early[1])),
        ]
    else:
        rest = [tile_term(standard, nb).astype(jnp.bfloat16) for nb in chained(standard)]
        totals = list(exchanged(jnp.stack([first] + rest)))
    kept = []
    for dist in range(TAPS):
        tile = totals[dist] / samples
        kept.append(jnp.where(dist <= own_reach, tile, jnp.zeros_like(tile)))
    return jnp.concatenate(kept, axis=1)


def solution(mesh):
    return jax.shard_map(
        local,
        mesh=mesh,
        in_specs=(P("smp", "snp"), P("snp")),
        out_specs=P(("snp", "smp"), None),
        check_vma=False,
    )
```

```python
import jax
import jax.numpy as jnp
from jax import lax
from jax.sharding import PartitionSpec as P

TAPS = 4


def shifted(value, axis, steps):
    count = lax.axis_size(axis)
    first, last = (max(0, -steps), min(count, count - steps))
    return lax.ppermute(value, axis, [(source, source + steps) for source in range(first, last)])


def rotated(value, axis, steps):
    count = lax.axis_size(axis)
    return lax.ppermute(value, axis, [(source, (source + steps) % count) for source in range(count)])


def chained(piece):
    out = []
    previous = piece
    for dist in range(1, TAPS):
        previous = shifted(previous, "snp", 1)
        out.append(previous)
    return out


def relayed(standard, count, place):
    def send(value, pairs):
        pairs = [(s, t) for s, t in pairs if 0 <= s < count and 0 <= t < count]
        return lax.ppermute(value, "snp", pairs)

    def pairs_of(*steps):
        return [(b + s, b + t) for b in range(0, count, 4) for s, t in steps]

    cross = send(standard, pairs_of((1, 2), (0, 3)))
    fast_a = send(standard, pairs_of((0, 1), (2, 3), (1, 4), (3, 6)))
    fast_b = send(standard, pairs_of((2, 1), (3, 2), (1, 0)))
    relay = send(fast_b, pairs_of((1, 4))) + send(fast_a, pairs_of((2, 1)))
    lhs = lax.optimization_barrier(jnp.where(place % 2 == 0, fast_b, fast_a))
    rhs = lax.optimization_barrier(relay + cross)
    handed = send(tile_term(lhs, rhs).astype(jnp.bfloat16), pairs_of((0, 1), (1, 0), (2, 3), (3, 2)))
    own_late = tile_term(standard, rhs).astype(jnp.bfloat16)
    with_a = tile_term(standard, fast_a).astype(jnp.bfloat16)
    return with_a, own_late, handed


def tile_term(standard, neighbour):
    return lax.dot_general(
        standard, neighbour, (((0,), (0,)), ((), ())), preferred_element_type=jnp.float32
    )


def local(dosage, reach):
    rows, width = dosage.shape
    n_smp = lax.axis_size("smp")
    samples = rows * n_smp
    me = lax.axis_index("smp")

    part_mean = jnp.sum(dosage, axis=0) / rows
    deviation = dosage - part_mean
    part_m2 = jnp.sum(deviation * deviation, axis=0)
    stats = jnp.stack([part_mean, part_m2])
    gathered = [stats] + [rotated(stats, "smp", s) for s in range(1, n_smp)]
    mean = gathered[0][0]
    for g in gathered[1:]:
        mean = mean + g[0]
    mean = mean / n_smp
    m2 = gathered[0][1]
    spread = (gathered[0][0] - mean) ** 2
    for g in gathered[1:]:
        m2 = m2 + g[1]
        spread = spread + (g[0] - mean) ** 2
    var = (m2 + rows * spread) / samples
    standard = ((dosage - mean) * lax.rsqrt(var + 1e-05)).astype(jnp.bfloat16)

    count = lax.axis_size("snp")
    share = width // n_smp
    own_reach = reach[0]
    first = tile_term(standard, standard).astype(jnp.bfloat16)

    def exchanged(partial):
        pieces = partial.reshape(partial.shape[:-2] + (n_smp, share, width))
        axis = pieces.ndim - 3
        total = lax.dynamic_index_in_dim(pieces, me, axis, keepdims=False).astype(jnp.float32)
        for s in range(1, n_smp):
            outgoing = lax.dynamic_index_in_dim(pieces, (me + s) % n_smp, axis, keepdims=False)
            total = total + rotated(outgoing, "smp", s).astype(jnp.float32)
        return total

    if count % 4 == 0:
        place = lax.axis_index("snp") % 4
        with_a, own_late, handed = relayed(standard, count, place)
        early = exchanged(jnp.stack([first, with_a]))
        late = [exchanged(own_late), exchanged(handed)]
        totals = [
            early[0],
            jnp.where(place == 0, late[1], jnp.where(place == 2, late[0], early[1])),
            jnp.where(place < 2, late[0], late[1]),
            jnp.where(place == 1, late[1], jnp.where(place == 3, late[0], early[1])),
        ]
    else:
        rest = [tile_term(standard, nb).astype(jnp.bfloat16) for nb in chained(standard)]
        totals = list(exchanged(jnp.stack([first] + rest)))
    kept = []
    for dist in range(TAPS):
        tile = totals[dist] / samples
        kept.append(jnp.where(dist <= own_reach, tile, jnp.zeros_like(tile)))
    return jnp.concatenate(kept, axis=1)


def solution(mesh):
    return jax.shard_map(
        local,
        mesh=mesh,
        in_specs=(P("smp", "snp"), P("snp")),
        out_specs=P(("snp", "smp"), None),
        check_vma=False,
    )
```

```python
import jax
import jax.numpy as jnp
from jax import lax
from jax.sharding import PartitionSpec as P

TAPS = 4


def shifted(value, axis, steps):
    count = lax.axis_size(axis)
    first, last = (max(0, -steps), min(count, count - steps))
    return lax.ppermute(value, axis, [(source, source + steps) for source in range(first, last)])


def rotated(value, axis, steps):
    count = lax.axis_size(axis)
    return lax.ppermute(value, axis, [(source, (source + steps) % count) for source in range(count)])


def chained(piece):
    out = []
    previous = piece
    for dist in range(1, TAPS):
        previous = shifted(previous, "snp", 1)
        out.append(previous)
    return out


def relayed(standard, count, place):
    def send(value, pairs):
        pairs = [(s, t) for s, t in pairs if 0 <= s < count and 0 <= t < count]
        return lax.ppermute(value, "snp", pairs)

    def pairs_of(*steps):
        return [(b + s, b + t) for b in range(0, count, 4) for s, t in steps]

    cross = send(standard, pairs_of((1, 2), (0, 3)))
    fast_a = send(standard, pairs_of((0, 1), (2, 3), (1, 4), (3, 6)))
    fast_b = send(standard, pairs_of((2, 1), (3, 2), (1, 0)))
    relay = send(fast_b, pairs_of((1, 4))) + send(fast_a, pairs_of((2, 1)))
    lhs = lax.optimization_barrier(jnp.where(place % 2 == 0, fast_b, fast_a))
    rhs = lax.optimization_barrier(relay + cross)
    handed = send(tile_term(lhs, rhs).astype(jnp.bfloat16), pairs_of((0, 1), (1, 0), (2, 3), (3, 2)))
    own_late = tile_term(standard, rhs).astype(jnp.bfloat16)
    with_a = tile_term(standard, fast_a).astype(jnp.bfloat16)
    return with_a, own_late, handed


def tile_term(standard, neighbour):
    return lax.dot_general(
        standard, neighbour, (((0,), (0,)), ((), ())), preferred_element_type=jnp.float32
    )


def local(dosage, reach):
    rows, width = dosage.shape
    n_smp = lax.axis_size("smp")
    samples = rows * n_smp
    me = lax.axis_index("smp")

    origin = dosage[0]
    shifted_dosage = dosage - origin
    part_sum = jnp.sum(shifted_dosage, axis=0)
    part_square = jnp.sum(shifted_dosage * shifted_dosage, axis=0)
    part_mean = origin + part_sum / rows
    part_m2 = part_square - part_sum * (part_sum / rows)
    stats = jnp.stack([part_mean, part_m2])
    gathered = [stats] + [rotated(stats, "smp", s) for s in range(1, n_smp)]
    mean = gathered[0][0]
    for g in gathered[1:]:
        mean = mean + g[0]
    mean = mean / n_smp
    m2 = gathered[0][1]
    spread = (gathered[0][0] - mean) ** 2
    for g in gathered[1:]:
        m2 = m2 + g[1]
        spread = spread + (g[0] - mean) ** 2
    var = (m2 + rows * spread) / samples
    standard = ((dosage - mean) * lax.rsqrt(var + 1e-05)).astype(jnp.bfloat16)

    count = lax.axis_size("snp")
    share = width // n_smp
    own_reach = reach[0]
    first = tile_term(standard, standard).astype(jnp.bfloat16)

    def exchanged(partial):
        pieces = partial.reshape(partial.shape[:-2] + (n_smp, share, width))
        axis = pieces.ndim - 3
        total = lax.dynamic_index_in_dim(pieces, me, axis, keepdims=False).astype(jnp.float32)
        for s in range(1, n_smp):
            outgoing = lax.dynamic_index_in_dim(pieces, (me + s) % n_smp, axis, keepdims=False)
            total = total + rotated(outgoing, "smp", s).astype(jnp.float32)
        return total

    if count % 4 == 0:
        place = lax.axis_index("snp") % 4
        with_a, own_late, handed = relayed(standard, count, place)
        early = exchanged(jnp.stack([first, with_a]))
        late = [exchanged(own_late), exchanged(handed)]
        totals = [
            early[0],
            jnp.where(place == 0, late[1], jnp.where(place == 2, late[0], early[1])),
            jnp.where(place < 2, late[0], late[1]),
            jnp.where(place == 1, late[1], jnp.where(place == 3, late[0], early[1])),
        ]
    else:
        rest = [tile_term(standard, nb).astype(jnp.bfloat16) for nb in chained(standard)]
        totals = list(exchanged(jnp.stack([first] + rest)))
    kept = []
    for dist in range(TAPS):
        tile = totals[dist] / samples
        kept.append(jnp.where(dist <= own_reach, tile, jnp.zeros_like(tile)))
    return jnp.concatenate(kept, axis=1)


def solution(mesh):
    return jax.shard_map(
        local,
        mesh=mesh,
        in_specs=(P("smp", "snp"), P("snp")),
        out_specs=P(("snp", "smp"), None),
        check_vma=False,
    )
```

```python
import jax
import jax.numpy as jnp
from jax import lax
from jax.sharding import PartitionSpec as P

TAPS = 4


def shifted(value, axis, steps):
    count = lax.axis_size(axis)
    first, last = (max(0, -steps), min(count, count - steps))
    return lax.ppermute(value, axis, [(source, source + steps) for source in range(first, last)])


def rotated(value, axis, steps):
    count = lax.axis_size(axis)
    return lax.ppermute(value, axis, [(source, (source + steps) % count) for source in range(count)])


def chained(piece):
    out = []
    previous = piece
    for dist in range(1, TAPS):
        previous = shifted(previous, "snp", 1)
        out.append(previous)
    return out


def relayed(standard, count, place, early_of):
    def send(value, pairs):
        pairs = [(s, t) for s, t in pairs if 0 <= s < count and 0 <= t < count]
        return lax.ppermute(value, "snp", pairs)

    def pairs_of(*steps):
        return [(b + s, b + t) for b in range(0, count, 4) for s, t in steps]

    cross = send(standard, pairs_of((1, 2), (0, 3)))
    fast_a = send(standard, pairs_of((0, 1), (2, 3), (1, 4), (3, 6)))
    fast_b = send(standard, pairs_of((2, 1), (3, 2), (1, 0)))
    relay = send(fast_b, pairs_of((1, 4))) + send(fast_a, pairs_of((2, 1)))
    width = standard.shape[1]
    early = early_of(tile_term(standard, fast_a).astype(jnp.bfloat16))
    both, early = lax.optimization_barrier(
        (jnp.concatenate([standard, jnp.where(place % 2 == 0, fast_b, fast_a)], axis=1), early)
    )
    rhs = lax.optimization_barrier(relay + cross)
    product = tile_term(both, rhs).astype(jnp.bfloat16)
    own_late = product[:width]
    handed = send(product[width:], pairs_of((0, 1), (1, 0), (2, 3), (3, 2)))
    return early, own_late, handed


def tile_term(standard, neighbour):
    return lax.dot_general(
        standard, neighbour, (((0,), (0,)), ((), ())), preferred_element_type=jnp.float32
    )


def local(dosage, reach):
    rows, width = dosage.shape
    n_smp = lax.axis_size("smp")
    samples = rows * n_smp
    me = lax.axis_index("smp")

    origin = dosage[0]
    shifted_dosage = dosage - origin
    part_sum = jnp.sum(shifted_dosage, axis=0)
    part_square = jnp.sum(shifted_dosage * shifted_dosage, axis=0)
    part_mean = origin + part_sum / rows
    part_m2 = part_square - part_sum * (part_sum / rows)
    stats = jnp.stack([part_mean, part_m2])
    gathered = [stats] + [rotated(stats, "smp", s) for s in range(1, n_smp)]
    mean = gathered[0][0]
    for g in gathered[1:]:
        mean = mean + g[0]
    mean = mean / n_smp
    m2 = gathered[0][1]
    spread = (gathered[0][0] - mean) ** 2
    for g in gathered[1:]:
        m2 = m2 + g[1]
        spread = spread + (g[0] - mean) ** 2
    var = (m2 + rows * spread) / samples
    standard = ((dosage - mean) * lax.rsqrt(var + 1e-05)).astype(jnp.bfloat16)

    count = lax.axis_size("snp")
    share = width // n_smp
    own_reach = reach[0]
    first = tile_term(standard, standard).astype(jnp.bfloat16)

    def exchanged(partial):
        pieces = partial.reshape(partial.shape[:-2] + (n_smp, share, width))
        axis = pieces.ndim - 3
        total = lax.dynamic_index_in_dim(pieces, me, axis, keepdims=False).astype(jnp.float32)
        for s in range(1, n_smp):
            outgoing = lax.dynamic_index_in_dim(pieces, (me + s) % n_smp, axis, keepdims=False)
            total = total + rotated(outgoing, "smp", s).astype(jnp.float32)
        return total

    if count % 4 == 0:
        place = lax.axis_index("snp") % 4
        early, own_late, handed = relayed(
            standard, count, place, lambda with_a: exchanged(jnp.stack([first, with_a]))
        )
        late = [exchanged(own_late), exchanged(handed)]
        totals = [
            early[0],
            jnp.where(place == 0, late[1], jnp.where(place == 2, late[0], early[1])),
            jnp.where(place < 2, late[0], late[1]),
            jnp.where(place == 1, late[1], jnp.where(place == 3, late[0], early[1])),
        ]
    else:
        rest = [tile_term(standard, nb).astype(jnp.bfloat16) for nb in chained(standard)]
        totals = list(exchanged(jnp.stack([first] + rest)))
    kept = []
    for dist in range(TAPS):
        tile = totals[dist] / samples
        kept.append(jnp.where(dist <= own_reach, tile, jnp.zeros_like(tile)))
    return jnp.concatenate(kept, axis=1)


def solution(mesh):
    return jax.shard_map(
        local,
        mesh=mesh,
        in_specs=(P("smp", "snp"), P("snp")),
        out_specs=P(("snp", "smp"), None),
        check_vma=False,
    )
```

```python
import jax
import jax.numpy as jnp
from jax import lax
from jax.sharding import PartitionSpec as P

TAPS = 4


def shifted(value, axis, steps):
    count = lax.axis_size(axis)
    first, last = (max(0, -steps), min(count, count - steps))
    return lax.ppermute(value, axis, [(source, source + steps) for source in range(first, last)])


def rotated(value, axis, steps):
    count = lax.axis_size(axis)
    return lax.ppermute(value, axis, [(source, (source + steps) % count) for source in range(count)])


def chained(piece):
    out = []
    previous = piece
    for dist in range(1, TAPS):
        previous = shifted(previous, "snp", 1)
        out.append(previous)
    return out


def relayed(standard, count, place, early_of):
    def send(value, pairs):
        pairs = [(s, t) for s, t in pairs if 0 <= s < count and 0 <= t < count]
        return lax.ppermute(value, "snp", pairs)

    def pairs_of(*steps):
        return [(b + s, b + t) for b in range(0, count, 4) for s, t in steps]

    cross = send(standard, pairs_of((1, 2), (0, 3)))
    fast_a = send(standard, pairs_of((0, 1), (2, 3), (1, 4), (3, 6)))
    fast_b = send(standard, pairs_of((2, 1), (3, 2), (1, 0)))
    relay = send(fast_b, pairs_of((1, 4))) + send(fast_a, pairs_of((2, 1)))
    width = standard.shape[1]
    early = early_of(tile_term(standard, fast_a).astype(jnp.bfloat16))
    both, early = lax.optimization_barrier(
        (jnp.concatenate([standard, jnp.where(place % 2 == 0, fast_b, fast_a)], axis=1), early)
    )
    rhs = lax.optimization_barrier(relay + cross)
    product = tile_term(both, rhs).astype(jnp.bfloat16)
    own_late = product[:width]
    handed = to_partner(product[width:], count)
    return early, own_late, handed


def to_partner(partial, count):
    n_smp = lax.axis_size("smp")
    me = lax.axis_index("smp")
    width = partial.shape[1]
    share = width // n_smp
    pieces = partial.reshape(n_smp, share, width)
    partners = [(b + s, b + t) for b in range(0, count, 4) for s, t in ((0, 1), (1, 0), (2, 3), (3, 2))]
    partners = [(s, t) for s, t in partners if t < count]
    total = lax.ppermute(
        lax.dynamic_index_in_dim(pieces, me, 0, keepdims=False), "snp", partners
    ).astype(jnp.float32)
    for step in range(1, n_smp):
        outgoing = lax.dynamic_index_in_dim(pieces, (me + step) % n_smp, 0, keepdims=False)
        pairs = [
            (s * n_smp + k, t * n_smp + (k + step) % n_smp) for s, t in partners for k in range(n_smp)
        ]
        total = total + lax.ppermute(outgoing, ("snp", "smp"), pairs).astype(jnp.float32)
    return total


def tile_term(standard, neighbour):
    return lax.dot_general(
        standard, neighbour, (((0,), (0,)), ((), ())), preferred_element_type=jnp.float32
    )


def local(dosage, reach):
    rows, width = dosage.shape
    n_smp = lax.axis_size("smp")
    samples = rows * n_smp
    me = lax.axis_index("smp")

    origin = dosage[0]
    shifted_dosage = dosage - origin
    part_sum = jnp.sum(shifted_dosage, axis=0)
    part_square = jnp.sum(shifted_dosage * shifted_dosage, axis=0)
    part_mean = origin + part_sum / rows
    part_m2 = part_square - part_sum * (part_sum / rows)
    stats = jnp.stack([part_mean, part_m2])
    gathered = [stats] + [rotated(stats, "smp", s) for s in range(1, n_smp)]
    mean = gathered[0][0]
    for g in gathered[1:]:
        mean = mean + g[0]
    mean = mean / n_smp
    m2 = gathered[0][1]
    spread = (gathered[0][0] - mean) ** 2
    for g in gathered[1:]:
        m2 = m2 + g[1]
        spread = spread + (g[0] - mean) ** 2
    var = (m2 + rows * spread) / samples
    standard = ((dosage - mean) * lax.rsqrt(var + 1e-05)).astype(jnp.bfloat16)

    count = lax.axis_size("snp")
    share = width // n_smp
    own_reach = reach[0]
    first = tile_term(standard, standard).astype(jnp.bfloat16)

    def exchanged(partial):
        pieces = partial.reshape(partial.shape[:-2] + (n_smp, share, width))
        axis = pieces.ndim - 3
        total = lax.dynamic_index_in_dim(pieces, me, axis, keepdims=False).astype(jnp.float32)
        for s in range(1, n_smp):
            outgoing = lax.dynamic_index_in_dim(pieces, (me + s) % n_smp, axis, keepdims=False)
            total = total + rotated(outgoing, "smp", s).astype(jnp.float32)
        return total

    if count % 4 == 0:
        place = lax.axis_index("snp") % 4
        early, own_late, handed = relayed(
            standard, count, place, lambda with_a: exchanged(jnp.stack([first, with_a]))
        )
        late = [exchanged(own_late), handed]
        totals = [
            early[0],
            jnp.where(place == 0, late[1], jnp.where(place == 2, late[0], early[1])),
            jnp.where(place < 2, late[0], late[1]),
            jnp.where(place == 1, late[1], jnp.where(place == 3, late[0], early[1])),
        ]
    else:
        rest = [tile_term(standard, nb).astype(jnp.bfloat16) for nb in chained(standard)]
        totals = list(exchanged(jnp.stack([first] + rest)))
    kept = []
    for dist in range(TAPS):
        tile = totals[dist] / samples
        kept.append(jnp.where(dist <= own_reach, tile, jnp.zeros_like(tile)))
    return jnp.concatenate(kept, axis=1)


def solution(mesh):
    return jax.shard_map(
        local,
        mesh=mesh,
        in_specs=(P("smp", "snp"), P("snp")),
        out_specs=P(("snp", "smp"), None),
        check_vma=False,
    )
```

```python
import jax
import jax.numpy as jnp
from jax import lax
from jax.sharding import PartitionSpec as P

TAPS = 4


def shifted(value, axis, steps):
    count = lax.axis_size(axis)
    first, last = (max(0, -steps), min(count, count - steps))
    return lax.ppermute(value, axis, [(source, source + steps) for source in range(first, last)])


def rotated(value, axis, steps):
    count = lax.axis_size(axis)
    return lax.ppermute(value, axis, [(source, (source + steps) % count) for source in range(count)])


def chained(piece):
    out = []
    previous = piece
    for dist in range(1, TAPS):
        previous = shifted(previous, "snp", 1)
        out.append(previous)
    return out


def relayed(standard, count, place, early_of):
    def send(value, pairs):
        pairs = [(s, t) for s, t in pairs if 0 <= s < count and 0 <= t < count]
        return lax.ppermute(value, "snp", pairs)

    def pairs_of(*steps):
        return [(b + s, b + t) for b in range(0, count, 4) for s, t in steps]

    cross = send(standard, pairs_of((1, 2), (0, 3)))
    fast_a = send(standard, pairs_of((0, 1), (2, 3), (1, 4), (3, 6)))
    fast_b = send(standard, pairs_of((2, 1), (3, 2), (1, 0)))
    relay = send(fast_b, pairs_of((1, 4))) + send(fast_a, pairs_of((2, 1)))
    width = standard.shape[1]
    early = early_of(tile_term(standard, fast_a).astype(jnp.bfloat16))
    both, early = lax.optimization_barrier(
        (jnp.concatenate([standard, jnp.where(place % 2 == 0, fast_b, fast_a)], axis=1), early)
    )
    rhs = lax.optimization_barrier(relay + cross)
    product = tile_term(both, rhs).astype(jnp.bfloat16)
    own_late = product[:width]
    handed = to_partner(product[width:], count)
    return early, own_late, handed


def to_partner(partial, count):
    n_smp = lax.axis_size("smp")
    me = lax.axis_index("smp")
    width = partial.shape[1]
    share = width // n_smp
    pieces = partial.reshape(n_smp, share, width)
    partners = [(b + s, b + t) for b in range(0, count, 4) for s, t in ((0, 1), (1, 0), (2, 3), (3, 2))]
    partners = [(s, t) for s, t in partners if t < count]
    total = lax.ppermute(
        lax.dynamic_index_in_dim(pieces, me, 0, keepdims=False), "snp", partners
    ).astype(jnp.float32)
    for step in range(1, n_smp):
        outgoing = lax.dynamic_index_in_dim(pieces, (me + step) % n_smp, 0, keepdims=False)
        pairs = [
            (s * n_smp + k, t * n_smp + (k + step) % n_smp) for s, t in partners for k in range(n_smp)
        ]
        total = total + lax.ppermute(outgoing, ("snp", "smp"), pairs).astype(jnp.float32)
    return total


def tile_term(standard, neighbour):
    return lax.dot_general(
        standard, neighbour, (((0,), (0,)), ((), ())), preferred_element_type=jnp.float32
    )


def local(dosage, reach):
    rows, width = dosage.shape
    n_smp = lax.axis_size("smp")
    samples = rows * n_smp
    me = lax.axis_index("smp")

    origin = dosage[0]
    shifted_dosage = dosage - origin
    part_sum = jnp.sum(shifted_dosage, axis=0)
    part_square = jnp.sum(shifted_dosage * shifted_dosage, axis=0)
    part_mean = origin + part_sum / rows
    part_m2 = part_square - part_sum * (part_sum / rows)
    stats = jnp.stack([part_mean, part_m2])
    gathered = [stats] + [rotated(stats, "smp", s) for s in range(1, n_smp)]
    mean = gathered[0][0]
    for g in gathered[1:]:
        mean = mean + g[0]
    mean = mean / n_smp
    m2 = gathered[0][1]
    spread = (gathered[0][0] - mean) ** 2
    for g in gathered[1:]:
        m2 = m2 + g[1]
        spread = spread + (g[0] - mean) ** 2
    var = (m2 + rows * spread) / samples
    standard = ((dosage - mean) * lax.rsqrt(var + 1e-05)).astype(jnp.bfloat16)

    count = lax.axis_size("snp")
    share = width // n_smp
    own_reach = reach[0]
    first = tile_term(standard, standard).astype(jnp.bfloat16)

    def exchanged(partial):
        pieces = partial.reshape(partial.shape[:-2] + (n_smp, share, width))
        axis = pieces.ndim - 3
        total = lax.dynamic_index_in_dim(pieces, me, axis, keepdims=False).astype(jnp.float32)
        for s in range(1, n_smp):
            outgoing = lax.dynamic_index_in_dim(pieces, (me + s) % n_smp, axis, keepdims=False)
            total = total + rotated(outgoing, "smp", s).astype(jnp.float32)
        return total

    if count % 4 == 0:
        place = lax.axis_index("snp") % 4
        early, own_late, handed = relayed(
            standard, count, place, lambda with_a: exchanged(jnp.stack([first, with_a]))
        )
        late_own = exchanged(own_late)

        def scaled(tile, dist):
            return jnp.where(dist <= own_reach, tile / samples, jnp.zeros_like(tile))

        odd = place % 2 == 1
        blank = jnp.zeros_like(early[0])
        out = jnp.concatenate(
            [
                scaled(early[0], 0),
                jnp.where(odd, scaled(early[1], 1), blank),
                blank,
                jnp.where(odd, blank, scaled(early[1], 3)),
            ],
            axis=1,
        )
        own_tap = jnp.where(place < 2, 2, jnp.where(place == 2, 1, 3))
        hand_tap = jnp.where(place == 0, 1, jnp.where(place == 1, 3, 2))
        out = lax.dynamic_update_slice(out, scaled(late_own, own_tap), (0, own_tap * width))
        return lax.dynamic_update_slice(out, scaled(handed, hand_tap), (0, hand_tap * width))
    else:
        rest = [tile_term(standard, nb).astype(jnp.bfloat16) for nb in chained(standard)]
        totals = list(exchanged(jnp.stack([first] + rest)))
    kept = []
    for dist in range(TAPS):
        tile = totals[dist] / samples
        kept.append(jnp.where(dist <= own_reach, tile, jnp.zeros_like(tile)))
    return jnp.concatenate(kept, axis=1)


def solution(mesh):
    return jax.shard_map(
        local,
        mesh=mesh,
        in_specs=(P("smp", "snp"), P("snp")),
        out_specs=P(("snp", "smp"), None),
        check_vma=False,
    )
```

```python
import jax
import jax.numpy as jnp
from jax import lax
from jax.sharding import PartitionSpec as P

TAPS = 4


def shifted(value, axis, steps):
    count = lax.axis_size(axis)
    first, last = (max(0, -steps), min(count, count - steps))
    return lax.ppermute(value, axis, [(source, source + steps) for source in range(first, last)])


def rotated(value, axis, steps):
    count = lax.axis_size(axis)
    return lax.ppermute(value, axis, [(source, (source + steps) % count) for source in range(count)])


def chained(piece):
    out = []
    previous = piece
    for dist in range(1, TAPS):
        previous = shifted(previous, "snp", 1)
        out.append(previous)
    return out


def relayed(standard, count, place, early_of):
    def send(value, pairs):
        pairs = [(s, t) for s, t in pairs if 0 <= s < count and 0 <= t < count]
        return lax.ppermute(value, "snp", pairs)

    def pairs_of(*steps):
        return [(b + s, b + t) for b in range(0, count, 4) for s, t in steps]

    fast_a = send(standard, pairs_of((0, 1), (2, 3), (1, 4), (3, 6)))
    fast_b = send(standard, pairs_of((2, 1), (3, 2), (1, 0)))
    width = standard.shape[1]
    half = width // 2

    def in_turn(value, pairs):
        first_half = send(value[:, :half], pairs)
        second_half = send(lax.optimization_barrier((value[:, half:], first_half))[0], pairs)
        return [first_half, second_half]

    cross = in_turn(standard, pairs_of((1, 2), (0, 3)))
    relay_b = in_turn(fast_b, pairs_of((1, 4)))
    relay_a = in_turn(fast_a, pairs_of((2, 1)))
    early = early_of(tile_term(standard, fast_a).astype(jnp.bfloat16))
    both, early = lax.optimization_barrier(
        (jnp.concatenate([standard, jnp.where(place % 2 == 0, fast_b, fast_a)], axis=1), early)
    )
    parts = []
    for piece in range(2):
        rhs = lax.optimization_barrier(relay_a[piece] + relay_b[piece] + cross[piece])
        product = tile_term(both, rhs).astype(jnp.bfloat16)
        parts.append((piece * half, product[:width], to_partner(product[width:], count)))
    return early, parts


def to_partner(partial, count):
    n_smp = lax.axis_size("smp")
    me = lax.axis_index("smp")
    share = partial.shape[0] // n_smp
    pieces = partial.reshape(n_smp, share, partial.shape[1])
    partners = [(b + s, b + t) for b in range(0, count, 4) for s, t in ((0, 1), (1, 0), (2, 3), (3, 2))]
    partners = [(s, t) for s, t in partners if t < count]
    total = lax.ppermute(
        lax.dynamic_index_in_dim(pieces, me, 0, keepdims=False), "snp", partners
    ).astype(jnp.float32)
    for step in range(1, n_smp):
        outgoing = lax.dynamic_index_in_dim(pieces, (me + step) % n_smp, 0, keepdims=False)
        pairs = [
            (s * n_smp + k, t * n_smp + (k + step) % n_smp) for s, t in partners for k in range(n_smp)
        ]
        total = total + lax.ppermute(outgoing, ("snp", "smp"), pairs).astype(jnp.float32)
    return total


def tile_term(standard, neighbour):
    return lax.dot_general(
        standard, neighbour, (((0,), (0,)), ((), ())), preferred_element_type=jnp.float32
    )


def local(dosage, reach):
    rows, width = dosage.shape
    n_smp = lax.axis_size("smp")
    samples = rows * n_smp
    me = lax.axis_index("smp")

    origin = dosage[0]
    shifted_dosage = dosage - origin
    part_sum = jnp.sum(shifted_dosage, axis=0)
    part_square = jnp.sum(shifted_dosage * shifted_dosage, axis=0)
    part_mean = origin + part_sum / rows
    part_m2 = part_square - part_sum * (part_sum / rows)
    stats = jnp.stack([part_mean, part_m2])
    gathered = [stats] + [rotated(stats, "smp", s) for s in range(1, n_smp)]
    mean = gathered[0][0]
    for g in gathered[1:]:
        mean = mean + g[0]
    mean = mean / n_smp
    m2 = gathered[0][1]
    spread = (gathered[0][0] - mean) ** 2
    for g in gathered[1:]:
        m2 = m2 + g[1]
        spread = spread + (g[0] - mean) ** 2
    var = (m2 + rows * spread) / samples
    standard = ((dosage - mean) * lax.rsqrt(var + 1e-05)).astype(jnp.bfloat16)

    count = lax.axis_size("snp")
    share = width // n_smp
    own_reach = reach[0]
    first = tile_term(standard, standard).astype(jnp.bfloat16)

    def exchanged(partial):
        pieces = partial.reshape(partial.shape[:-2] + (n_smp, share, partial.shape[-1]))
        axis = pieces.ndim - 3
        total = lax.dynamic_index_in_dim(pieces, me, axis, keepdims=False).astype(jnp.float32)
        for s in range(1, n_smp):
            outgoing = lax.dynamic_index_in_dim(pieces, (me + s) % n_smp, axis, keepdims=False)
            total = total + rotated(outgoing, "smp", s).astype(jnp.float32)
        return total

    if count % 4 == 0:
        place = lax.axis_index("snp") % 4
        early, parts = relayed(
            standard, count, place, lambda with_a: exchanged(jnp.stack([first, with_a]))
        )
        def scaled(tile, dist):
            return jnp.where(dist <= own_reach, tile / samples, jnp.zeros_like(tile))

        odd = place % 2 == 1
        blank = jnp.zeros_like(early[0])
        out = jnp.concatenate(
            [
                scaled(early[0], 0),
                jnp.where(odd, scaled(early[1], 1), blank),
                blank,
                jnp.where(odd, blank, scaled(early[1], 3)),
            ],
            axis=1,
        )
        own_tap = jnp.where(place < 2, 2, jnp.where(place == 2, 1, 3))
        hand_tap = jnp.where(place == 0, 1, jnp.where(place == 1, 3, 2))
        for offset, own_late, handed in parts:
            late_own = exchanged(own_late)
            out = lax.dynamic_update_slice(out, scaled(late_own, own_tap), (0, own_tap * width + offset))
            out = lax.dynamic_update_slice(out, scaled(handed, hand_tap), (0, hand_tap * width + offset))
        return out
    else:
        rest = [tile_term(standard, nb).astype(jnp.bfloat16) for nb in chained(standard)]
        totals = list(exchanged(jnp.stack([first] + rest)))
    kept = []
    for dist in range(TAPS):
        tile = totals[dist] / samples
        kept.append(jnp.where(dist <= own_reach, tile, jnp.zeros_like(tile)))
    return jnp.concatenate(kept, axis=1)


def solution(mesh):
    return jax.shard_map(
        local,
        mesh=mesh,
        in_specs=(P("smp", "snp"), P("snp")),
        out_specs=P(("snp", "smp"), None),
        check_vma=False,
    )
```

```python
import jax
import jax.numpy as jnp
from jax import lax
from jax.sharding import PartitionSpec as P

TAPS = 4


def shifted(value, axis, steps):
    count = lax.axis_size(axis)
    first, last = (max(0, -steps), min(count, count - steps))
    return lax.ppermute(value, axis, [(source, source + steps) for source in range(first, last)])


def rotated(value, axis, steps):
    count = lax.axis_size(axis)
    return lax.ppermute(value, axis, [(source, (source + steps) % count) for source in range(count)])


def chained(piece):
    out = []
    previous = piece
    for dist in range(1, TAPS):
        previous = shifted(previous, "snp", 1)
        out.append(previous)
    return out


def relayed(standard, count, place, early_of):
    def send(value, pairs):
        pairs = [(s, t) for s, t in pairs if 0 <= s < count and 0 <= t < count]
        return lax.ppermute(value, "snp", pairs)

    def pairs_of(*steps):
        return [(b + s, b + t) for b in range(0, count, 4) for s, t in steps]

    fast_a = send(standard, pairs_of((0, 1), (2, 3), (1, 4), (3, 6)))
    fast_b = send(standard, pairs_of((2, 1), (3, 2), (1, 0)))
    width = standard.shape[1]
    half = width // 2

    def in_turn(value, pairs):
        first_half = send(value[:, :half], pairs)
        held = lax.optimization_barrier((value[:, half:], first_half, fast_a, fast_b))[0]
        return [first_half, send(held, pairs)]

    cross = in_turn(standard, pairs_of((1, 2), (0, 3)))
    relay_b = in_turn(fast_b, pairs_of((1, 4)))
    relay_a = in_turn(fast_a, pairs_of((2, 1)))
    early = early_of(tile_term(standard, fast_a).astype(jnp.bfloat16))
    both, early = lax.optimization_barrier(
        (jnp.concatenate([standard, jnp.where(place % 2 == 0, fast_b, fast_a)], axis=1), early)
    )
    parts = []
    for piece in range(2):
        rhs = lax.optimization_barrier(relay_a[piece] + relay_b[piece] + cross[piece])
        product = tile_term(both, rhs).astype(jnp.bfloat16)
        parts.append((piece * half, product[:width], to_partner(product[width:], count)))
    return early, parts


def to_partner(partial, count):
    n_smp = lax.axis_size("smp")
    me = lax.axis_index("smp")
    share = partial.shape[0] // n_smp
    pieces = partial.reshape(n_smp, share, partial.shape[1])
    partners = [(b + s, b + t) for b in range(0, count, 4) for s, t in ((0, 1), (1, 0), (2, 3), (3, 2))]
    partners = [(s, t) for s, t in partners if t < count]
    total = lax.ppermute(
        lax.dynamic_index_in_dim(pieces, me, 0, keepdims=False), "snp", partners
    ).astype(jnp.float32)
    for step in range(1, n_smp):
        outgoing = lax.dynamic_index_in_dim(pieces, (me + step) % n_smp, 0, keepdims=False)
        pairs = [
            (s * n_smp + k, t * n_smp + (k + step) % n_smp) for s, t in partners for k in range(n_smp)
        ]
        total = total + lax.ppermute(outgoing, ("snp", "smp"), pairs).astype(jnp.float32)
    return total


def tile_term(standard, neighbour):
    return lax.dot_general(
        standard, neighbour, (((0,), (0,)), ((), ())), preferred_element_type=jnp.float32
    )


def local(dosage, reach):
    rows, width = dosage.shape
    n_smp = lax.axis_size("smp")
    samples = rows * n_smp
    me = lax.axis_index("smp")

    origin = dosage[0]
    shifted_dosage = dosage - origin
    part_sum = jnp.sum(shifted_dosage, axis=0)
    part_square = jnp.sum(shifted_dosage * shifted_dosage, axis=0)
    part_mean = origin + part_sum / rows
    part_m2 = part_square - part_sum * (part_sum / rows)
    stats = jnp.stack([part_mean, part_m2])
    gathered = [stats] + [rotated(stats, "smp", s) for s in range(1, n_smp)]
    mean = gathered[0][0]
    for g in gathered[1:]:
        mean = mean + g[0]
    mean = mean / n_smp
    m2 = gathered[0][1]
    spread = (gathered[0][0] - mean) ** 2
    for g in gathered[1:]:
        m2 = m2 + g[1]
        spread = spread + (g[0] - mean) ** 2
    var = (m2 + rows * spread) / samples
    standard = ((dosage - mean) * lax.rsqrt(var + 1e-05)).astype(jnp.bfloat16)

    count = lax.axis_size("snp")
    share = width // n_smp
    own_reach = reach[0]
    first = tile_term(standard, standard).astype(jnp.bfloat16)

    def exchanged(partial):
        pieces = partial.reshape(partial.shape[:-2] + (n_smp, share, partial.shape[-1]))
        axis = pieces.ndim - 3
        total = lax.dynamic_index_in_dim(pieces, me, axis, keepdims=False).astype(jnp.float32)
        for s in range(1, n_smp):
            outgoing = lax.dynamic_index_in_dim(pieces, (me + s) % n_smp, axis, keepdims=False)
            total = total + rotated(outgoing, "smp", s).astype(jnp.float32)
        return total

    if count % 4 == 0:
        place = lax.axis_index("snp") % 4
        early, parts = relayed(
            standard, count, place, lambda with_a: exchanged(jnp.stack([first, with_a]))
        )
        def scaled(tile, dist):
            return jnp.where(dist <= own_reach, tile / samples, jnp.zeros_like(tile))

        odd = place % 2 == 1
        blank = jnp.zeros_like(early[0])
        out = jnp.concatenate(
            [
                scaled(early[0], 0),
                jnp.where(odd, scaled(early[1], 1), blank),
                blank,
                jnp.where(odd, blank, scaled(early[1], 3)),
            ],
            axis=1,
        )
        own_tap = jnp.where(place < 2, 2, jnp.where(place == 2, 1, 3))
        hand_tap = jnp.where(place == 0, 1, jnp.where(place == 1, 3, 2))
        for offset, own_late, handed in parts:
            late_own = exchanged(own_late)
            out = lax.dynamic_update_slice(out, scaled(late_own, own_tap), (0, own_tap * width + offset))
            out = lax.dynamic_update_slice(out, scaled(handed, hand_tap), (0, hand_tap * width + offset))
        return out
    else:
        rest = [tile_term(standard, nb).astype(jnp.bfloat16) for nb in chained(standard)]
        totals = list(exchanged(jnp.stack([first] + rest)))
    kept = []
    for dist in range(TAPS):
        tile = totals[dist] / samples
        kept.append(jnp.where(dist <= own_reach, tile, jnp.zeros_like(tile)))
    return jnp.concatenate(kept, axis=1)


def solution(mesh):
    return jax.shard_map(
        local,
        mesh=mesh,
        in_specs=(P("smp", "snp"), P("snp")),
        out_specs=P(("snp", "smp"), None),
        check_vma=False,
    )
```

```python
import jax
import jax.numpy as jnp
from jax import lax
from jax.sharding import PartitionSpec as P

TAPS = 4


def shifted(value, axis, steps):
    count = lax.axis_size(axis)
    first, last = (max(0, -steps), min(count, count - steps))
    return lax.ppermute(value, axis, [(source, source + steps) for source in range(first, last)])


def rotated(value, axis, steps):
    count = lax.axis_size(axis)
    return lax.ppermute(value, axis, [(source, (source + steps) % count) for source in range(count)])


def chained(piece):
    out = []
    previous = piece
    for dist in range(1, TAPS):
        previous = shifted(previous, "snp", 1)
        out.append(previous)
    return out


def relayed(standard, count, place, early_of):
    def send(value, pairs):
        pairs = [(s, t) for s, t in pairs if 0 <= s < count and 0 <= t < count]
        return lax.ppermute(value, "snp", pairs)

    def pairs_of(*steps):
        return [(b + s, b + t) for b in range(0, count, 4) for s, t in steps]

    cross = send(standard, pairs_of((1, 2), (0, 3), (3, 5)))
    fast_a = send(standard, pairs_of((0, 1), (2, 3), (1, 4), (3, 6)))
    fast_b = send(standard, pairs_of((2, 1), (3, 2), (1, 0)))
    relay = send(fast_b, pairs_of((1, 4)))
    width = standard.shape[1]
    early = early_of(tile_term(standard, fast_a).astype(jnp.bfloat16))
    both, early = lax.optimization_barrier(
        (jnp.concatenate([standard, jnp.where(place % 2 == 0, fast_b, fast_a)], axis=1), early)
    )
    rhs = lax.optimization_barrier(relay + cross)
    product = tile_term(both, rhs).astype(jnp.bfloat16)
    own_late = product[:width]
    handed = to_partner(product[width:], count)
    return early, own_late, handed


def to_partner(partial, count):
    n_smp = lax.axis_size("smp")
    me = lax.axis_index("smp")
    width = partial.shape[1]
    share = width // n_smp
    pieces = partial.reshape(n_smp, share, width)
    partners = [(b + s, b + t) for b in range(0, count, 4) for s, t in ((0, 1), (1, 0), (2, 3), (3, 2))]
    partners = [(s, t) for s, t in partners if t < count]
    total = lax.ppermute(
        lax.dynamic_index_in_dim(pieces, me, 0, keepdims=False), "snp", partners
    ).astype(jnp.float32)
    for step in range(1, n_smp):
        outgoing = lax.dynamic_index_in_dim(pieces, (me + step) % n_smp, 0, keepdims=False)
        pairs = [
            (s * n_smp + k, t * n_smp + (k + step) % n_smp) for s, t in partners for k in range(n_smp)
        ]
        total = total + lax.ppermute(outgoing, ("snp", "smp"), pairs).astype(jnp.float32)
    return total


def tile_term(standard, neighbour):
    return lax.dot_general(
        standard, neighbour, (((0,), (0,)), ((), ())), preferred_element_type=jnp.float32
    )


def local(dosage, reach):
    rows, width = dosage.shape
    n_smp = lax.axis_size("smp")
    samples = rows * n_smp
    me = lax.axis_index("smp")

    origin = dosage[0]
    shifted_dosage = dosage - origin
    part_sum = jnp.sum(shifted_dosage, axis=0)
    part_square = jnp.sum(shifted_dosage * shifted_dosage, axis=0)
    part_mean = origin + part_sum / rows
    part_m2 = part_square - part_sum * (part_sum / rows)
    stats = jnp.stack([part_mean, part_m2])
    gathered = [stats] + [rotated(stats, "smp", s) for s in range(1, n_smp)]
    mean = gathered[0][0]
    for g in gathered[1:]:
        mean = mean + g[0]
    mean = mean / n_smp
    m2 = gathered[0][1]
    spread = (gathered[0][0] - mean) ** 2
    for g in gathered[1:]:
        m2 = m2 + g[1]
        spread = spread + (g[0] - mean) ** 2
    var = (m2 + rows * spread) / samples
    standard = ((dosage - mean) * lax.rsqrt(var + 1e-05)).astype(jnp.bfloat16)

    count = lax.axis_size("snp")
    share = width // n_smp
    own_reach = reach[0]
    first = tile_term(standard, standard).astype(jnp.bfloat16)

    def exchanged(partial):
        pieces = partial.reshape(partial.shape[:-2] + (n_smp, share, width))
        axis = pieces.ndim - 3
        total = lax.dynamic_index_in_dim(pieces, me, axis, keepdims=False).astype(jnp.float32)
        for s in range(1, n_smp):
            outgoing = lax.dynamic_index_in_dim(pieces, (me + s) % n_smp, axis, keepdims=False)
            total = total + rotated(outgoing, "smp", s).astype(jnp.float32)
        return total

    if count % 4 == 0:
        place = lax.axis_index("snp") % 4
        early, own_late, handed = relayed(
            standard, count, place, lambda with_a: exchanged(jnp.stack([first, with_a]))
        )
        late_own = exchanged(own_late)

        def scaled(tile, dist):
            return jnp.where(dist <= own_reach, tile / samples, jnp.zeros_like(tile))

        odd = place % 2 == 1
        blank = jnp.zeros_like(early[0])
        out = jnp.concatenate(
            [
                scaled(early[0], 0),
                jnp.where(odd, scaled(early[1], 1), blank),
                blank,
                jnp.where(odd, blank, scaled(early[1], 3)),
            ],
            axis=1,
        )
        own_tap = jnp.where(place < 2, 2, jnp.where(place == 2, 1, 3))
        hand_tap = jnp.where(place == 0, 1, jnp.where(place == 1, 3, 2))
        out = lax.dynamic_update_slice(out, scaled(late_own, own_tap), (0, own_tap * width))
        return lax.dynamic_update_slice(out, scaled(handed, hand_tap), (0, hand_tap * width))
    else:
        rest = [tile_term(standard, nb).astype(jnp.bfloat16) for nb in chained(standard)]
        totals = list(exchanged(jnp.stack([first] + rest)))
    kept = []
    for dist in range(TAPS):
        tile = totals[dist] / samples
        kept.append(jnp.where(dist <= own_reach, tile, jnp.zeros_like(tile)))
    return jnp.concatenate(kept, axis=1)


def solution(mesh):
    return jax.shard_map(
        local,
        mesh=mesh,
        in_specs=(P("smp", "snp"), P("snp")),
        out_specs=P(("snp", "smp"), None),
        check_vma=False,
    )
```

```python
import jax
import jax.numpy as jnp
from jax import lax
from jax.sharding import PartitionSpec as P

TAPS = 4


def shifted(value, axis, steps):
    count = lax.axis_size(axis)
    first, last = (max(0, -steps), min(count, count - steps))
    return lax.ppermute(value, axis, [(source, source + steps) for source in range(first, last)])


def rotated(value, axis, steps):
    count = lax.axis_size(axis)
    return lax.ppermute(value, axis, [(source, (source + steps) % count) for source in range(count)])


def chained(piece):
    out = []
    previous = piece
    for dist in range(1, TAPS):
        previous = shifted(previous, "snp", 1)
        out.append(previous)
    return out


def relayed(standard, count, place, early_of):
    def send(value, pairs):
        pairs = [(s, t) for s, t in pairs if 0 <= s < count and 0 <= t < count]
        return lax.ppermute(value, "snp", pairs)

    def pairs_of(*steps):
        return [(b + s, b + t) for b in range(0, count, 4) for s, t in steps]

    cross = send(standard, pairs_of((1, 2), (0, 3)))
    fast_a = send(standard, pairs_of((0, 1), (2, 3), (1, 4), (3, 6)))
    fast_b = send(standard, pairs_of((2, 1), (3, 2), (1, 0)))
    relay = send(fast_b, pairs_of((1, 4))) + send(fast_a, pairs_of((2, 1)))
    width = standard.shape[1]
    early = early_of(tile_term(standard, fast_a).astype(jnp.bfloat16))
    both, early = lax.optimization_barrier(
        (jnp.concatenate([standard, jnp.where(place % 2 == 0, fast_b, fast_a)], axis=1), early)
    )
    rhs = lax.optimization_barrier(relay + cross)
    product = tile_term(both, rhs).astype(jnp.bfloat16)
    own_late = product[:width]
    handed = to_partner(product[width:], count)
    return early, own_late, handed


def to_partner(partial, count):
    n_smp = lax.axis_size("smp")
    me = lax.axis_index("smp")
    width = partial.shape[1]
    share = width // n_smp
    pieces = partial.reshape(n_smp, share, width)
    partners = [(b + s, b + t) for b in range(0, count, 4) for s, t in ((0, 1), (1, 0), (2, 3), (3, 2))]
    partners = [(s, t) for s, t in partners if t < count]
    total = lax.ppermute(
        lax.dynamic_index_in_dim(pieces, me, 0, keepdims=False), "snp", partners
    ).astype(jnp.float32)
    for step in range(1, n_smp):
        outgoing = lax.dynamic_index_in_dim(pieces, (me + step) % n_smp, 0, keepdims=False)
        pairs = [
            (s * n_smp + k, t * n_smp + (k + step) % n_smp) for s, t in partners for k in range(n_smp)
        ]
        total = total + lax.ppermute(outgoing, ("snp", "smp"), pairs).astype(jnp.float32)
    return total


def tile_term(standard, neighbour):
    return lax.dot_general(
        standard, neighbour, (((0,), (0,)), ((), ())), preferred_element_type=jnp.float32
    )


def local(dosage, reach):
    rows, width = dosage.shape
    n_smp = lax.axis_size("smp")
    samples = rows * n_smp
    me = lax.axis_index("smp")

    origin = dosage[0]
    shifted_dosage = dosage - origin
    groups = 16 if rows % 128 == 0 else 1
    grouped = shifted_dosage.reshape(groups, rows // groups, width)
    part_sum, part_square = lax.optimization_barrier(
        (jnp.sum(grouped, axis=1), jnp.sum(grouped * grouped, axis=1))
    )
    part_sum = jnp.sum(part_sum, axis=0)
    part_square = jnp.sum(part_square, axis=0)
    part_mean = origin + part_sum / rows
    part_m2 = part_square - part_sum * (part_sum / rows)
    stats = jnp.stack([part_mean, part_m2])
    gathered = [stats] + [rotated(stats, "smp", s) for s in range(1, n_smp)]
    mean = gathered[0][0]
    for g in gathered[1:]:
        mean = mean + g[0]
    mean = mean / n_smp
    m2 = gathered[0][1]
    spread = (gathered[0][0] - mean) ** 2
    for g in gathered[1:]:
        m2 = m2 + g[1]
        spread = spread + (g[0] - mean) ** 2
    var = (m2 + rows * spread) / samples
    standard = ((dosage - mean) * lax.rsqrt(var + 1e-05)).astype(jnp.bfloat16)

    count = lax.axis_size("snp")
    share = width // n_smp
    own_reach = reach[0]
    first = tile_term(standard, standard).astype(jnp.bfloat16)

    def exchanged(partial):
        pieces = partial.reshape(partial.shape[:-2] + (n_smp, share, width))
        axis = pieces.ndim - 3
        total = lax.dynamic_index_in_dim(pieces, me, axis, keepdims=False).astype(jnp.float32)
        for s in range(1, n_smp):
            outgoing = lax.dynamic_index_in_dim(pieces, (me + s) % n_smp, axis, keepdims=False)
            total = total + rotated(outgoing, "smp", s).astype(jnp.float32)
        return total

    if count % 4 == 0:
        place = lax.axis_index("snp") % 4
        early, own_late, handed = relayed(
            standard, count, place, lambda with_a: exchanged(jnp.stack([first, with_a]))
        )
        late_own = exchanged(own_late)

        def scaled(tile, dist):
            return jnp.where(dist <= own_reach, tile / samples, jnp.zeros_like(tile))

        odd = place % 2 == 1
        blank = jnp.zeros_like(early[0])
        out = jnp.concatenate(
            [
                scaled(early[0], 0),
                jnp.where(odd, scaled(early[1], 1), blank),
                blank,
                jnp.where(odd, blank, scaled(early[1], 3)),
            ],
            axis=1,
        )
        own_tap = jnp.where(place < 2, 2, jnp.where(place == 2, 1, 3))
        hand_tap = jnp.where(place == 0, 1, jnp.where(place == 1, 3, 2))
        out = lax.dynamic_update_slice(out, scaled(late_own, own_tap), (0, own_tap * width))
        return lax.dynamic_update_slice(out, scaled(handed, hand_tap), (0, hand_tap * width))
    else:
        rest = [tile_term(standard, nb).astype(jnp.bfloat16) for nb in chained(standard)]
        totals = list(exchanged(jnp.stack([first] + rest)))
    kept = []
    for dist in range(TAPS):
        tile = totals[dist] / samples
        kept.append(jnp.where(dist <= own_reach, tile, jnp.zeros_like(tile)))
    return jnp.concatenate(kept, axis=1)


def solution(mesh):
    return jax.shard_map(
        local,
        mesh=mesh,
        in_specs=(P("smp", "snp"), P("snp")),
        out_specs=P(("snp", "smp"), None),
        check_vma=False,
    )
```

```python
import jax
import jax.numpy as jnp
from jax import lax
from jax.sharding import PartitionSpec as P

TAPS = 4


def shifted(value, axis, steps):
    count = lax.axis_size(axis)
    first, last = (max(0, -steps), min(count, count - steps))
    return lax.ppermute(value, axis, [(source, source + steps) for source in range(first, last)])


def rotated(value, axis, steps):
    count = lax.axis_size(axis)
    return lax.ppermute(value, axis, [(source, (source + steps) % count) for source in range(count)])


def chained(piece):
    out = []
    previous = piece
    for dist in range(1, TAPS):
        previous = shifted(previous, "snp", 1)
        out.append(previous)
    return out


def relayed(standard, count, place, early_of):
    def send(value, pairs):
        pairs = [(s, t) for s, t in pairs if 0 <= s < count and 0 <= t < count]
        return lax.ppermute(value, "snp", pairs)

    def pairs_of(*steps):
        return [(b + s, b + t) for b in range(0, count, 4) for s, t in steps]

    cross = send(standard, pairs_of((1, 2), (0, 3), (2, 4), (3, 5)))
    fast_a = send(standard, pairs_of((0, 1), (2, 3), (1, 4), (3, 6)))
    fast_b = send(standard, pairs_of((3, 2), (1, 0)))
    width = standard.shape[1]
    early = early_of(tile_term(standard, fast_a).astype(jnp.bfloat16))
    both, early = lax.optimization_barrier(
        (jnp.concatenate([standard, jnp.where(place % 2 == 0, fast_b, fast_a)], axis=1), early)
    )
    rhs = lax.optimization_barrier(cross)
    product = tile_term(both, rhs).astype(jnp.bfloat16)
    own_late = product[:width]
    handed = to_partner(product[width:], count)
    return early, own_late, handed


def to_partner(partial, count):
    n_smp = lax.axis_size("smp")
    me = lax.axis_index("smp")
    width = partial.shape[1]
    share = width // n_smp
    pieces = partial.reshape(n_smp, share, width)
    partners = [(b + s, b + t) for b in range(0, count, 4) for s, t in ((0, 1), (1, 0), (2, 3), (3, 2))]
    partners = [(s, t) for s, t in partners if t < count]
    total = lax.ppermute(
        lax.dynamic_index_in_dim(pieces, me, 0, keepdims=False), "snp", partners
    ).astype(jnp.float32)
    for step in range(1, n_smp):
        outgoing = lax.dynamic_index_in_dim(pieces, (me + step) % n_smp, 0, keepdims=False)
        pairs = [
            (s * n_smp + k, t * n_smp + (k + step) % n_smp) for s, t in partners for k in range(n_smp)
        ]
        total = total + lax.ppermute(outgoing, ("snp", "smp"), pairs).astype(jnp.float32)
    return total


def tile_term(standard, neighbour):
    return lax.dot_general(
        standard, neighbour, (((0,), (0,)), ((), ())), preferred_element_type=jnp.float32
    )


def local(dosage, reach):
    rows, width = dosage.shape
    n_smp = lax.axis_size("smp")
    samples = rows * n_smp
    me = lax.axis_index("smp")

    origin = dosage[0]
    shifted_dosage = dosage - origin
    part_sum = jnp.sum(shifted_dosage, axis=0)
    part_square = jnp.sum(shifted_dosage * shifted_dosage, axis=0)
    part_mean = origin + part_sum / rows
    part_m2 = part_square - part_sum * (part_sum / rows)
    stats = jnp.stack([part_mean, part_m2])
    gathered = [stats] + [rotated(stats, "smp", s) for s in range(1, n_smp)]
    mean = gathered[0][0]
    for g in gathered[1:]:
        mean = mean + g[0]
    mean = mean / n_smp
    m2 = gathered[0][1]
    spread = (gathered[0][0] - mean) ** 2
    for g in gathered[1:]:
        m2 = m2 + g[1]
        spread = spread + (g[0] - mean) ** 2
    var = (m2 + rows * spread) / samples
    standard = ((dosage - mean) * lax.rsqrt(var + 1e-05)).astype(jnp.bfloat16)

    count = lax.axis_size("snp")
    share = width // n_smp
    own_reach = reach[0]
    first = tile_term(standard, standard).astype(jnp.bfloat16)

    def exchanged(partial):
        pieces = partial.reshape(partial.shape[:-2] + (n_smp, share, width))
        axis = pieces.ndim - 3
        total = lax.dynamic_index_in_dim(pieces, me, axis, keepdims=False).astype(jnp.float32)
        for s in range(1, n_smp):
            outgoing = lax.dynamic_index_in_dim(pieces, (me + s) % n_smp, axis, keepdims=False)
            total = total + rotated(outgoing, "smp", s).astype(jnp.float32)
        return total

    if count % 4 == 0:
        place = lax.axis_index("snp") % 4
        early, own_late, handed = relayed(
            standard, count, place, lambda with_a: exchanged(jnp.stack([first, with_a]))
        )
        late_own = exchanged(own_late)

        def scaled(tile, dist):
            return jnp.where(dist <= own_reach, tile / samples, jnp.zeros_like(tile))

        odd = place % 2 == 1
        blank = jnp.zeros_like(early[0])
        out = jnp.concatenate(
            [
                scaled(early[0], 0),
                jnp.where(odd, scaled(early[1], 1), blank),
                blank,
                jnp.where(odd, blank, scaled(early[1], 3)),
            ],
            axis=1,
        )
        own_tap = jnp.where(place < 2, 2, jnp.where(place == 2, 1, 3))
        hand_tap = jnp.where(place == 0, 1, jnp.where(place == 1, 3, 2))
        out = lax.dynamic_update_slice(out, scaled(late_own, own_tap), (0, own_tap * width))
        return lax.dynamic_update_slice(out, scaled(handed, hand_tap), (0, hand_tap * width))
    else:
        rest = [tile_term(standard, nb).astype(jnp.bfloat16) for nb in chained(standard)]
        totals = list(exchanged(jnp.stack([first] + rest)))
    kept = []
    for dist in range(TAPS):
        tile = totals[dist] / samples
        kept.append(jnp.where(dist <= own_reach, tile, jnp.zeros_like(tile)))
    return jnp.concatenate(kept, axis=1)


def solution(mesh):
    return jax.shard_map(
        local,
        mesh=mesh,
        in_specs=(P("smp", "snp"), P("snp")),
        out_specs=P(("snp", "smp"), None),
        check_vma=False,
    )
```
